512 devices in a mesh: pole: 2 (over core), prow: 16 (over z), pcol: 16 (over x, y).
Axes of the slice: x: 4, y: 4, z: 16, core: 2. Of those that a mesh axis runs over, the one named last changes fastest.
Arguments:
- inverse_trailing: float32 [32768, 16384], P(('pole', 'prow'), 'pcol'), parts along dimension 0, may hold values from -6 to 6
- factor_blocks: float32 [6, 4096, 256], P('pole', 'prow'), parts along dimension 0, may hold values from -0.09375 to 0.09375
- diag_pivots: float32 [256, 6, 256], P('pcol', 'pole'), parts along dimension 1, may hold values from -6 to 6
- structure: int32 [3, 16], replicated, may hold values from 0 to 63, as said below
- owner_map: int32 [64], replicated, may hold values from 0 to 63, each once
Outputs:
- row_inverse: float32 [256, 6, 16384], P('pcol', 'pole', 'prow'), parts along dimension 1
- diag_inverse: float32 [256, 6, 256], P('pcol', 'pole'), parts along dimension 1
The draws below stay inside these ranges and needn't reach their ends.
There are 2 independent parts, one for each index of `pole`. The reference program is written for one: setup_inputs(seed, part) draws one part's arguments, and reference() takes and returns one part's arrays. A program takes and returns all parts, laid end to end along the dimension named above; an argument that names none is the same for every part. Nothing has to cross between parts.
Inputs may be any that keep to these rules, and one draw needn't show every extreme that they name: `structure`: each row lists 16 distinct logical ancestor blocks.
All inputs are finite; a program needn't handle non-finite values.
Results may differ from the reference program's by a relative error of at most 0.0001.
Values sent between devices are 32-bit elements; how exact they have to be, the bound alone decides.
No kernel may reach another device: no remote copies, remote signals or barrier semaphores. Data moves between devices by JAX's collectives and lax.ppermute only.
A program may use at most 64 MiB of HBM per device.

```python
import jax
import jax.numpy as jnp
from jax import lax

BLOCK_WIDTH = 256
WINDOW = 3
ANCESTORS = 64
LISTED = 16


def draw_structure(key, part):
    keys = jax.random.split(jax.random.fold_in(key, 11), WINDOW)
    listed = jax.vmap(lambda single: jax.random.permutation(single, ANCESTORS)[:LISTED])(keys)
    return listed.astype(jnp.int32)


def block_scale(own_key, extent, cuts, low, top_value):
    level = 1.0
    for dim, parts in cuts:
        steps = jax.random.uniform(jax.random.fold_in(jax.random.fold_in(own_key, 6), dim), (parts,), jnp.float32, low / len(cuts), top_value / len(cuts))
        level = level * jnp.repeat(jnp.exp(steps), extent[dim] // parts).reshape((-1,) + (1,) * (len(extent) - 1 - dim))
    return level


def gaussian(key, dims, spread, reach, cuts=(), kind=jnp.bfloat16):
    drawn = spread * jax.random.normal(key, dims, jnp.float32)
    if cuts:
        drawn = drawn * block_scale(key, dims, cuts, -0.22, 0.18)
    return jnp.clip(drawn, -reach, reach).astype(kind)


def setup_inputs(seed: int = 0, part: int = 0) -> dict:
    key_of = jax.random.split(jax.random.key(seed), 6)
    part_keys = jax.random.split(jax.random.fold_in(key_of[5], part), 6)
    inverse_trailing = gaussian(part_keys[0], (ANCESTORS * BLOCK_WIDTH, ANCESTORS * BLOCK_WIDTH), 1.0, 6.0, ((0, 16), (1, 16)), jnp.float32)
    factor_blocks = gaussian(part_keys[1], (WINDOW, LISTED * BLOCK_WIDTH, BLOCK_WIDTH), (LISTED * BLOCK_WIDTH) ** -0.5, 0.09375, ((1, 16),), jnp.float32)
    diag_pivots = gaussian(part_keys[2], (BLOCK_WIDTH, WINDOW, BLOCK_WIDTH), 1.0, 6.0, ((0, 16),), jnp.float32)
    structure = draw_structure(jax.random.fold_in(key_of[5], 71), part)
    owner_map = jax.random.permutation(key_of[4], ANCESTORS).astype(jnp.int32)
    return {"inverse_trailing": inverse_trailing, "factor_blocks": factor_blocks, "diag_pivots": diag_pivots, "structure": structure, "owner_map": owner_map}


def reference(inverse_trailing, factor_blocks, diag_pivots, structure, owner_map):
    positions = owner_map[structure].astype(jnp.int32)
    trail = inverse_trailing.reshape(ANCESTORS, BLOCK_WIDTH, ANCESTORS, BLOCK_WIDTH)
    rows_list = []
    diag_list = []
    for index in range(WINDOW):
        where = positions[index]
        picked = jnp.take(jnp.take(trail, where, axis=0), where, axis=2)
        factor = factor_blocks[index].reshape(LISTED, BLOCK_WIDTH, BLOCK_WIDTH)
        part_rows = -jnp.einsum("irjc,jca->air", picked, factor, precision=lax.Precision.HIGHEST)
        filled = jnp.zeros((BLOCK_WIDTH, ANCESTORS, BLOCK_WIDTH), part_rows.dtype).at[:, where, :].set(part_rows)
        rows_list.append(filled.reshape(BLOCK_WIDTH, ANCESTORS * BLOCK_WIDTH))
        reduced = jnp.einsum("air,irb->ab", part_rows, factor, precision=lax.Precision.HIGHEST)
        diag_list.append(diag_pivots[:, index, :] - reduced)
    return jnp.stack(rows_list, axis=1), jnp.stack(diag_list, axis=1)
```

```python
import jax
import jax.numpy as jnp
from jax import lax
from jax.sharding import PartitionSpec as P


def diag_product(values, factor):
    return jnp.einsum("awj,wjb->awb", values, factor, precision=lax.Precision.HIGHEST)


def pick_blocks(blocks, positions, slots):
    window = blocks.shape[0]
    match = positions[:, None, :] == slots[None, :, None]
    index = jnp.argmax(match, axis=2)
    present = jnp.any(match, axis=2)
    chosen = blocks[jnp.arange(window)[:, None], index]
    return jnp.where(present[:, :, None, None], chosen, 0.0), present


def make_shards(prow_size, pcol_size):
    def shards(inverse_trailing, factor_blocks, diag_pivots, structure, owner_map):
        width = factor_blocks.shape[2]
        window = factor_blocks.shape[0]
        local_rows = factor_blocks.shape[1]
        owned = inverse_trailing.shape[0] // width
        row_index = lax.axis_index("prow")
        col_index = lax.axis_index("pcol")
        positions = jnp.take(owner_map, structure, axis=0)
        slots = jnp.arange(owned, dtype=jnp.int32)
        col_slots = col_index * owned + slots
        row_slots = row_index * owned + slots
        segment = local_rows // pcol_size
        mine = lax.dynamic_slice_in_dim(factor_blocks, col_index * segment, segment, axis=1)
        piece = lax.all_gather(mine, ("prow", "pcol"), axis=1, tiled=True)
        count = piece.shape[1] // width
        blocks = piece.reshape(window, count, width, width)
        col_acc, _ = pick_blocks(blocks, positions, col_slots)
        row_acc, in_rows = pick_blocks(blocks, positions, row_slots)
        col_factor = col_acc.reshape(window, owned * width, width)
        row_factor = row_acc.reshape(window, owned * width, width)
        row_mask = jnp.repeat(in_rows.astype(jnp.float32), width, axis=1)
        summed = lax.psum_scatter(
            -jnp.einsum("wja,ij->awi", col_factor, inverse_trailing, precision=lax.Precision.HIGHEST),
            "pcol",
            scatter_dimension=0,
            tiled=True,
        )
        row_inverse = summed * row_mask[None, :, :]
        local_diag = diag_product(row_inverse, row_factor)
        gathered = lax.all_gather(local_diag, "prow", axis=0, tiled=False)
        total_diag = jnp.sum(gathered, axis=0)
        diag_inverse = diag_pivots - total_diag
        return (row_inverse, diag_inverse)

    return shards


def solution(mesh):
    in_specs = (
        P(("pole", "prow"), "pcol"),
        P("pole", "prow", None),
        P("pcol", "pole", None),
        P(),
        P(),
    )
    out_specs = (P("pcol", "pole", "prow"), P("pcol", "pole", None))
    shards = make_shards(mesh.shape["prow"], mesh.shape["pcol"])
    return jax.shard_map(shards, mesh=mesh, in_specs=in_specs, out_specs=out_specs, check_vma=False)
```

```python
import jax
import jax.numpy as jnp
from jax import lax
from jax.sharding import PartitionSpec as P


def diag_product(values, factor):
    return jnp.einsum("awj,wjb->awb", values, factor, precision=lax.Precision.HIGHEST)


def slot_lookup(positions, slots):
    match = positions[:, None, :] == slots[None, :, None]
    return jnp.argmax(match, axis=2), jnp.any(match, axis=2)


def make_shards(prow_size, pcol_size):
    def shards(inverse_trailing, factor_blocks, diag_pivots, structure, owner_map):
        width = factor_blocks.shape[2]
        window = factor_blocks.shape[0]
        local_rows = factor_blocks.shape[1]
        owned = inverse_trailing.shape[0] // width
        row_index = lax.axis_index("prow")
        col_index = lax.axis_index("pcol")
        positions = jnp.take(owner_map, structure, axis=0)
        slots = jnp.arange(owned, dtype=jnp.int32)
        segment = local_rows // pcol_size
        mine = lax.dynamic_slice_in_dim(factor_blocks, col_index * segment, segment, axis=1)
        pieces = lax.all_gather(mine, "prow", axis=1, tiled=True)
        count = pieces.shape[1] // segment
        pieces = pieces.reshape(window, count, segment, width)
        windows = jnp.arange(window)
        dest_slots = jnp.arange(pcol_size, dtype=jnp.int32)[:, None] * owned + slots[None, :]
        dest_index, dest_present = jax.vmap(lambda s: slot_lookup(positions, s))(dest_slots)
        send = pieces[windows[None, :, None], dest_index]
        send = jnp.where(dest_present[..., None, None], send, 0.0)
        send = jnp.transpose(send, (1, 2, 0, 3, 4))
        received = lax.all_to_all(send, "pcol", 2, 2, tiled=True)
        col_factor = received.reshape(window, owned * local_rows, width)
        row_index_map, in_rows = slot_lookup(positions, row_index * owned + slots)
        row_piece = pieces[windows[:, None], row_index_map]
        row_piece = jnp.where(in_rows[..., None, None], row_piece, 0.0)
        row_factor = lax.all_gather(row_piece, "pcol", axis=2, tiled=True)
        row_factor = row_factor.reshape(window, owned * width, width)
        row_mask = jnp.repeat(in_rows.astype(jnp.float32), width, axis=1)
        partial = -jnp.einsum("wja,ij->awi", col_factor, inverse_trailing, precision=lax.Precision.HIGHEST)
        share = partial.shape[0] // pcol_size
        partial = partial.reshape((pcol_size, share) + partial.shape[1:])
        summed = jnp.sum(lax.all_to_all(partial, "pcol", 0, 0, tiled=True), axis=0)
        row_inverse = summed * row_mask[None, :, :]
        local_diag = diag_product(row_inverse, row_factor)
        gathered = lax.all_gather(local_diag, "prow", axis=0, tiled=False)
        total_diag = jnp.sum(gathered, axis=0)
        diag_inverse = diag_pivots - total_diag
        return (row_inverse, diag_inverse)

    return shards


def solution(mesh):
    in_specs = (
        P(("pole", "prow"), "pcol"),
        P("pole", "prow", None),
        P("pcol", "pole", None),
        P(),
        P(),
    )
    out_specs = (P("pcol", "pole", "prow"), P("pcol", "pole", None))
    shards = make_shards(mesh.shape["prow"], mesh.shape["pcol"])
    return jax.shard_map(shards, mesh=mesh, in_specs=in_specs, out_specs=out_specs, check_vma=False)
```

```python
import jax
import jax.numpy as jnp
from jax import lax
from jax.sharding import PartitionSpec as P


def diag_product(values, factor):
    return jnp.einsum("awj,wjb->awb", values, factor, precision=lax.Precision.HIGHEST)


def slot_lookup(positions, slots):
    match = positions[:, None, :] == slots[None, :, None]
    return jnp.argmax(match, axis=2), jnp.any(match, axis=2)


def butterfly_gather(x, axis_name, size):
    index = lax.axis_index(axis_name)
    held = x[None]
    step = 1
    while step < size:
        other = lax.ppermute(held, axis_name, perm=[(i, i ^ step) for i in range(size)])
        lower = (index & step) == 0
        held = jnp.where(lower, jnp.concatenate([held, other], 0), jnp.concatenate([other, held], 0))
        step *= 2
    return held


def butterfly_sum(x, axis_name, size):
    step = 1
    while step < size:
        x = x + lax.ppermute(x, axis_name, perm=[(i, i ^ step) for i in range(size)])
        step *= 2
    return x


def make_shards(prow_size, pcol_size):
    def shards(inverse_trailing, factor_blocks, diag_pivots, structure, owner_map):
        width = factor_blocks.shape[2]
        window = factor_blocks.shape[0]
        local_rows = factor_blocks.shape[1]
        owned = inverse_trailing.shape[0] // width
        row_index = lax.axis_index("prow")
        col_index = lax.axis_index("pcol")
        positions = jnp.take(owner_map, structure, axis=0)
        slots = jnp.arange(owned, dtype=jnp.int32)
        segment = local_rows // pcol_size
        mine = lax.dynamic_slice_in_dim(factor_blocks, col_index * segment, segment, axis=1)
        pieces = butterfly_gather(mine, "prow", prow_size)
        pieces = jnp.transpose(pieces, (1, 0, 2, 3))
        windows = jnp.arange(window)
        dest_slots = jnp.arange(pcol_size, dtype=jnp.int32)[:, None] * owned + slots[None, :]
        dest_index, dest_present = jax.vmap(lambda s: slot_lookup(positions, s))(dest_slots)
        send = pieces[windows[None, :, None], dest_index]
        send = jnp.where(dest_present[..., None, None], send, 0.0)
        send = jnp.transpose(send, (1, 2, 0, 3, 4))
        received = lax.all_to_all(send, "pcol", 2, 2, tiled=True)
        col_factor = received.reshape(window, owned * local_rows, width)
        row_index_map, in_rows = slot_lookup(positions, row_index * owned + slots)
        row_piece = pieces[windows[:, None], row_index_map]
        row_piece = jnp.where(in_rows[..., None, None], row_piece, 0.0)
        row_factor = lax.all_gather(row_piece, "pcol", axis=2, tiled=True)
        row_factor = row_factor.reshape(window, owned * width, width)
        row_mask = jnp.repeat(in_rows.astype(jnp.float32), width, axis=1)
        partial = -jnp.einsum("wja,ij->awi", col_factor, inverse_trailing, precision=lax.Precision.HIGHEST)
        share = partial.shape[0] // pcol_size
        partial = partial.reshape((pcol_size, share) + partial.shape[1:])
        summed = jnp.sum(lax.all_to_all(partial, "pcol", 0, 0, tiled=True), axis=0)
        row_inverse = summed * row_mask[None, :, :]
        local_diag = diag_product(row_inverse, row_factor)
        total_diag = butterfly_sum(local_diag, "prow", prow_size)
        diag_inverse = diag_pivots - total_diag
        return (row_inverse, diag_inverse)

    return shards


def solution(mesh):
    in_specs = (
        P(("pole", "prow"), "pcol"),
        P("pole", "prow", None),
        P("pcol", "pole", None),
        P(),
        P(),
    )
    out_specs = (P("pcol", "pole", "prow"), P("pcol", "pole", None))
    shards = make_shards(mesh.shape["prow"], mesh.shape["pcol"])
    return jax.shard_map(shards, mesh=mesh, in_specs=in_specs, out_specs=out_specs, check_vma=False)
```

```python
import jax
import jax.numpy as jnp
from jax import lax
from jax.sharding import PartitionSpec as P


def diag_product(values, factor):
    return jnp.einsum("awj,wjb->awb", values, factor, precision=lax.Precision.HIGHEST)


def slot_lookup(positions, slots):
    match = positions[:, None, :] == slots[None, :, None]
    return jnp.argmax(match, axis=2), jnp.any(match, axis=2)


def make_shards(prow_size, pcol_size):
    def shards(inverse_trailing, factor_blocks, diag_pivots, structure, owner_map):
        width = factor_blocks.shape[2]
        window = factor_blocks.shape[0]
        local_rows = factor_blocks.shape[1]
        owned = inverse_trailing.shape[0] // width
        row_index = lax.axis_index("prow")
        col_index = lax.axis_index("pcol")
        positions = jnp.take(owner_map, structure, axis=0)
        slots = jnp.arange(owned, dtype=jnp.int32)
        segment = local_rows // pcol_size
        mine = lax.dynamic_slice_in_dim(factor_blocks, col_index * segment, segment, axis=1)
        pieces = lax.all_gather(mine, "prow", axis=1, tiled=True)
        count = pieces.shape[1] // segment
        pieces = pieces.reshape(window, count, segment, width)
        windows = jnp.arange(window)
        dest_slots = jnp.arange(pcol_size, dtype=jnp.int32)[:, None] * owned + slots[None, :]
        dest_index, dest_present = jax.vmap(lambda s: slot_lookup(positions, s))(dest_slots)
        send = pieces[windows[None, :, None], dest_index]
        send = jnp.where(dest_present[..., None, None], send, 0.0)
        send = jnp.transpose(send, (1, 2, 0, 3, 4))
        received = lax.all_to_all(send, "pcol", 2, 2, tiled=True)
        col_factor = received.reshape(window, owned * local_rows, width)
        row_index_map, in_rows = slot_lookup(positions, row_index * owned + slots)
        row_piece = pieces[windows[:, None], row_index_map]
        row_piece = jnp.where(in_rows[..., None, None], row_piece, 0.0)
        row_factor = lax.all_gather(row_piece, "pcol", axis=2, tiled=True)
        row_factor = row_factor.reshape(window, owned * width, width)
        row_mask = jnp.repeat(in_rows.astype(jnp.float32), width, axis=1)
        partial = -jnp.einsum("wja,ij->awi", col_factor, inverse_trailing, precision=lax.Precision.HIGH)
        share = partial.shape[0] // pcol_size
        partial = partial.reshape((pcol_size, share) + partial.shape[1:])
        summed = jnp.sum(lax.all_to_all(partial, "pcol", 0, 0, tiled=True), axis=0)
        row_inverse = summed * row_mask[None, :, :]
        local_diag = diag_product(row_inverse, row_factor)
        gathered = lax.all_gather(local_diag, "prow", axis=0, tiled=False)
        total_diag = jnp.sum(gathered, axis=0)
        diag_inverse = diag_pivots - total_diag
        return (row_inverse, diag_inverse)

    return shards


def solution(mesh):
    in_specs = (
        P(("pole", "prow"), "pcol"),
        P("pole", "prow", None),
        P("pcol", "pole", None),
        P(),
        P(),
    )
    out_specs = (P("pcol", "pole", "prow"), P("pcol", "pole", None))
    shards = make_shards(mesh.shape["prow"], mesh.shape["pcol"])
    return jax.shard_map(shards, mesh=mesh, in_specs=in_specs, out_specs=out_specs, check_vma=False)
```

```python
import functools

import jax
import jax.numpy as jnp
from jax import lax
from jax.sharding import PartitionSpec as P


def diag_product(values, factor):
    return jnp.einsum("awj,wjb->awb", values, factor, precision=lax.Precision.HIGHEST)


def slot_lookup(positions, slots):
    match = positions[:, None, :] == slots[None, :, None]
    return jnp.argmax(match, axis=2), jnp.any(match, axis=2)


PACKED = (6, 8, 12)


def pack_order(present, size):
    rank = jnp.cumsum(present.astype(jnp.int32), axis=1) - 1
    target = jnp.arange(size, dtype=jnp.int32)
    hit = present[:, None, :] & (rank[:, None, :] == target[None, :, None])
    return jnp.argmax(hit, axis=2).astype(jnp.int32), jnp.any(hit, axis=2)


def make_shards(prow_size, pcol_size):
    def shards(inverse_trailing, factor_blocks, diag_pivots, structure, owner_map):
        width = factor_blocks.shape[2]
        window = factor_blocks.shape[0]
        local_rows = factor_blocks.shape[1]
        owned = inverse_trailing.shape[0] // width
        row_index = lax.axis_index("prow")
        col_index = lax.axis_index("pcol")
        positions = jnp.take(owner_map, structure, axis=0)
        slots = jnp.arange(owned, dtype=jnp.int32)
        segment = local_rows // pcol_size
        mine = lax.dynamic_slice_in_dim(factor_blocks, col_index * segment, segment, axis=1)
        pieces = lax.all_gather(mine, "prow", axis=1, tiled=True)
        count = pieces.shape[1] // segment
        pieces = pieces.reshape(window, count, segment, width)
        windows = jnp.arange(window)
        flat_slots = window * owned
        dest_slots = jnp.arange(pcol_size, dtype=jnp.int32)[:, None] * owned + slots[None, :]
        dest_index, dest_present = jax.vmap(lambda s: slot_lookup(positions, s))(dest_slots)
        dest_index = dest_index.reshape(pcol_size, flat_slots)
        dest_present = dest_present.reshape(pcol_size, flat_slots)
        row_index_map, in_rows = slot_lookup(positions, row_index * owned + slots)
        row_piece = pieces[windows[:, None], row_index_map]
        row_piece = jnp.where(in_rows[..., None, None], row_piece, 0.0)
        row_factor = lax.all_gather(row_piece, "pcol", axis=2, tiled=True)
        row_factor = row_factor.reshape(window, owned * width, width)
        needed = jnp.max(jnp.sum(dest_present.astype(jnp.int32), axis=1))
        branch = jnp.sum((needed > jnp.array(PACKED[:-1], jnp.int32)).astype(jnp.int32))

        def route(size, pieces):
            send_slot, send_valid = pack_order(dest_present, size)
            send_w = send_slot // owned
            send_j = jnp.take_along_axis(dest_index, send_slot, axis=1)
            send = pieces[send_w, send_j]
            send = jnp.where(send_valid[..., None, None], send, 0.0)
            received = lax.all_to_all(send, "pcol", 0, 0, tiled=True)
            blocks = jnp.transpose(received, (1, 0, 2, 3)).reshape(size, local_rows, width)
            mine = dest_present[col_index]
            rank = jnp.clip(jnp.cumsum(mine.astype(jnp.int32)) - 1, 0, size - 1)
            return jnp.where(mine[:, None, None], blocks[rank], 0.0)

        def reduce_rows(size, partial):
            pair_slot, _ = pack_order(listed[None, :], size)
            chosen = jnp.take(partial, pair_slot[0], axis=1)
            share = chosen.shape[0] // pcol_size
            chosen = chosen.reshape((pcol_size, share) + chosen.shape[1:])
            summed = jnp.sum(lax.all_to_all(chosen, "pcol", 0, 0, tiled=True), axis=0)
            pair_rank = jnp.clip(jnp.cumsum(listed.astype(jnp.int32)) - 1, 0, size - 1)
            return jnp.where(listed[None, :, None], jnp.take(summed, pair_rank, axis=1), 0.0)

        listed = in_rows.reshape(flat_slots)
        col_factor = lax.switch(branch, [functools.partial(route, size) for size in PACKED], pieces)
        col_factor = col_factor.reshape(window, owned * local_rows, width)
        partial = -jnp.einsum("wja,ij->awi", col_factor, inverse_trailing, precision=lax.Precision.HIGHEST)
        partial = partial.reshape(partial.shape[0], flat_slots, width)
        rows = lax.switch(branch, [functools.partial(reduce_rows, size) for size in PACKED], partial)
        row_inverse = rows.reshape(rows.shape[0], window, owned * width)
        local_diag = diag_product(row_inverse, row_factor)
        gathered = lax.all_gather(local_diag, "prow", axis=0, tiled=False)
        total_diag = jnp.sum(gathered, axis=0)
        diag_inverse = diag_pivots - total_diag
        return (row_inverse, diag_inverse)

    return shards


def solution(mesh):
    in_specs = (
        P(("pole", "prow"), "pcol"),
        P("pole", "prow", None),
        P("pcol", "pole", None),
        P(),
        P(),
    )
    out_specs = (P("pcol", "pole", "prow"), P("pcol", "pole", None))
    shards = make_shards(mesh.shape["prow"], mesh.shape["pcol"])
    return jax.shard_map(shards, mesh=mesh, in_specs=in_specs, out_specs=out_specs, check_vma=False)
```

```python
import functools

import jax
import jax.numpy as jnp
from jax import lax
from jax.sharding import PartitionSpec as P


def diag_product(values, factor):
    return jnp.einsum("awj,wjb->awb", values, factor, precision=lax.Precision.HIGHEST)


def slot_lookup(positions, slots):
    match = positions[:, None, :] == slots[None, :, None]
    return jnp.argmax(match, axis=2), jnp.any(match, axis=2)


PACKED = (6, 8, 12)


def pack_order(present, size):
    rank = jnp.cumsum(present.astype(jnp.int32), axis=1) - 1
    target = jnp.arange(size, dtype=jnp.int32)
    hit = present[:, None, :] & (rank[:, None, :] == target[None, :, None])
    return jnp.argmax(hit, axis=2).astype(jnp.int32), jnp.any(hit, axis=2)


def make_shards(prow_size, pcol_size):
    def shards(inverse_trailing, factor_blocks, diag_pivots, structure, owner_map):
        width = factor_blocks.shape[2]
        window = factor_blocks.shape[0]
        local_rows = factor_blocks.shape[1]
        owned = inverse_trailing.shape[0] // width
        row_index = lax.axis_index("prow")
        col_index = lax.axis_index("pcol")
        positions = jnp.take(owner_map, structure, axis=0)
        slots = jnp.arange(owned, dtype=jnp.int32)
        segment = local_rows // pcol_size
        mine = lax.dynamic_slice_in_dim(factor_blocks, col_index * segment, segment, axis=1)
        pieces = lax.all_gather(mine, "prow", axis=1, tiled=True)
        count = pieces.shape[1] // segment
        pieces = pieces.reshape(window, count, segment, width)
        windows = jnp.arange(window)
        flat_slots = window * owned
        dest_slots = jnp.arange(pcol_size, dtype=jnp.int32)[:, None] * owned + slots[None, :]
        dest_index, dest_present = jax.vmap(lambda s: slot_lookup(positions, s))(dest_slots)
        dest_index = dest_index.reshape(pcol_size, flat_slots)
        dest_present = dest_present.reshape(pcol_size, flat_slots)
        row_index_map, in_rows = slot_lookup(positions, row_index * owned + slots)
        row_piece = pieces[windows[:, None], row_index_map]
        row_piece = jnp.where(in_rows[..., None, None], row_piece, 0.0)
        row_factor = lax.all_gather(row_piece, "pcol", axis=2, tiled=True)
        row_factor = row_factor.reshape(window, owned * width, width)
        needed = jnp.max(jnp.sum(dest_present.astype(jnp.int32), axis=1))
        branch = jnp.sum((needed > jnp.array(PACKED[:-1], jnp.int32)).astype(jnp.int32))

        def route(size, pieces):
            send_slot, send_valid = pack_order(dest_present, size)
            send_w = send_slot // owned
            send_j = jnp.take_along_axis(dest_index, send_slot, axis=1)
            send = pieces[send_w, send_j]
            send = jnp.where(send_valid[..., None, None], send, 0.0)
            received = lax.all_to_all(send, "pcol", 0, 0, tiled=True)
            blocks = jnp.transpose(received, (1, 0, 2, 3)).reshape(size, local_rows, width)
            mine = dest_present[col_index]
            rank = jnp.clip(jnp.cumsum(mine.astype(jnp.int32)) - 1, 0, size - 1)
            return jnp.where(mine[:, None, None], blocks[rank], 0.0)

        def reduce_rows(size, col_factor, inverse_trailing):
            pair_slot, _ = pack_order(listed[None, :], size)
            pair_slot = pair_slot[0]
            trail_rows = inverse_trailing.reshape(owned, width, -1)[pair_slot % owned]
            factor = col_factor[pair_slot // owned]
            chosen = jnp.einsum("ska,sik->asi", factor, trail_rows, precision=lax.Precision.HIGHEST)
            share = chosen.shape[0] // pcol_size
            chosen = chosen.reshape((pcol_size, share) + chosen.shape[1:])
            summed = jnp.sum(lax.all_to_all(chosen, "pcol", 0, 0, tiled=True), axis=0)
            pair_rank = jnp.clip(jnp.cumsum(listed.astype(jnp.int32)) - 1, 0, size - 1)
            return jnp.where(listed[None, :, None], -jnp.take(summed, pair_rank, axis=1), 0.0)

        listed = in_rows.reshape(flat_slots)
        col_factor = lax.switch(branch, [functools.partial(route, size) for size in PACKED], pieces)
        col_factor = col_factor.reshape(window, owned * local_rows, width)
        rows = lax.switch(
            branch, [functools.partial(reduce_rows, size) for size in PACKED], col_factor, inverse_trailing
        )
        row_inverse = rows.reshape(rows.shape[0], window, owned * width)
        local_diag = diag_product(row_inverse, row_factor)
        gathered = lax.all_gather(local_diag, "prow", axis=0, tiled=False)
        total_diag = jnp.sum(gathered, axis=0)
        diag_inverse = diag_pivots - total_diag
        return (row_inverse, diag_inverse)

    return shards


def solution(mesh):
    in_specs = (
        P(("pole", "prow"), "pcol"),
        P("pole", "prow", None),
        P("pcol", "pole", None),
        P(),
        P(),
    )
    out_specs = (P("pcol", "pole", "prow"), P("pcol", "pole", None))
    shards = make_shards(mesh.shape["prow"], mesh.shape["pcol"])
    return jax.shard_map(shards, mesh=mesh, in_specs=in_specs, out_specs=out_specs, check_vma=False)
```

```python
import functools

import jax
import jax.numpy as jnp
from jax import lax
from jax.sharding import PartitionSpec as P


def diag_product(values, factor):
    return jnp.einsum("awj,wjb->awb", values, factor, precision=lax.Precision.HIGHEST)


def slot_lookup(positions, slots):
    match = positions[:, None, :] == slots[None, :, None]
    return jnp.argmax(match, axis=2), jnp.any(match, axis=2)


PACKED = (5, 6, 7, 8, 12)


def pack_order(present, size):
    rank = jnp.cumsum(present.astype(jnp.int32), axis=1) - 1
    target = jnp.arange(size, dtype=jnp.int32)
    hit = present[:, None, :] & (rank[:, None, :] == target[None, :, None])
    return jnp.argmax(hit, axis=2).astype(jnp.int32), jnp.any(hit, axis=2)


def make_shards(prow_size, pcol_size):
    def shards(inverse_trailing, factor_blocks, diag_pivots, structure, owner_map):
        width = factor_blocks.shape[2]
        window = factor_blocks.shape[0]
        local_rows = factor_blocks.shape[1]
        owned = inverse_trailing.shape[0] // width
        row_index = lax.axis_index("prow")
        col_index = lax.axis_index("pcol")
        positions = jnp.take(owner_map, structure, axis=0)
        slots = jnp.arange(owned, dtype=jnp.int32)
        segment = local_rows // pcol_size
        mine = lax.dynamic_slice_in_dim(factor_blocks, col_index * segment, segment, axis=1)
        pieces = lax.all_gather(mine, "prow", axis=1, tiled=True)
        count = pieces.shape[1] // segment
        pieces = pieces.reshape(window, count, segment, width)
        windows = jnp.arange(window)
        flat_slots = window * owned
        dest_slots = jnp.arange(pcol_size, dtype=jnp.int32)[:, None] * owned + slots[None, :]
        dest_index, dest_present = jax.vmap(lambda s: slot_lookup(positions, s))(dest_slots)
        dest_index = dest_index.reshape(pcol_size, flat_slots)
        dest_present = dest_present.reshape(pcol_size, flat_slots)
        row_index_map, in_rows = slot_lookup(positions, row_index * owned + slots)
        row_piece = pieces[windows[:, None], row_index_map]
        row_piece = jnp.where(in_rows[..., None, None], row_piece, 0.0)
        row_factor = lax.all_gather(row_piece, "pcol", axis=2, tiled=True)
        row_factor = row_factor.reshape(window, owned * width, width)
        needed = jnp.max(jnp.sum(dest_present.astype(jnp.int32), axis=1))
        branch = jnp.sum((needed > jnp.array(PACKED[:-1], jnp.int32)).astype(jnp.int32))

        def route(size, pieces):
            send_slot, send_valid = pack_order(dest_present, size)
            send_w = send_slot // owned
            send_j = jnp.take_along_axis(dest_index, send_slot, axis=1)
            send = pieces[send_w, send_j]
            send = jnp.where(send_valid[..., None, None], send, 0.0)
            received = lax.all_to_all(send, "pcol", 0, 0, tiled=True)
            blocks = jnp.transpose(received, (1, 0, 2, 3)).reshape(size, local_rows, width)
            mine = dest_present[col_index]
            rank = jnp.clip(jnp.cumsum(mine.astype(jnp.int32)) - 1, 0, size - 1)
            return jnp.where(mine[:, None, None], blocks[rank], 0.0)

        def reduce_rows(size, partial):
            pair_slot, _ = pack_order(listed[None, :], size)
            chosen = jnp.take(partial, pair_slot[0], axis=1)
            share = chosen.shape[0] // pcol_size
            chosen = chosen.reshape((pcol_size, share) + chosen.shape[1:])
            summed = jnp.sum(lax.all_to_all(chosen, "pcol", 0, 0, tiled=True), axis=0)
            pair_rank = jnp.clip(jnp.cumsum(listed.astype(jnp.int32)) - 1, 0, size - 1)
            return jnp.where(listed[None, :, None], -jnp.take(summed, pair_rank, axis=1), 0.0)

        listed = in_rows.reshape(flat_slots)
        col_factor = lax.switch(branch, [functools.partial(route, size) for size in PACKED], pieces)
        col_factor = col_factor.reshape(window, owned * local_rows, width)
        partial = jnp.einsum("wja,ij->awi", col_factor, inverse_trailing, precision=lax.Precision.HIGHEST)
        partial = partial.reshape(partial.shape[0], flat_slots, width)
        rows = lax.switch(branch, [functools.partial(reduce_rows, size) for size in PACKED], partial)
        row_inverse = rows.reshape(rows.shape[0], window, owned * width)
        local_diag = diag_product(row_inverse, row_factor)
        gathered = lax.all_gather(local_diag, "prow", axis=0, tiled=False)
        total_diag = jnp.sum(gathered, axis=0)
        diag_inverse = diag_pivots - total_diag
        return (row_inverse, diag_inverse)

    return shards


def solution(mesh):
    in_specs = (
        P(("pole", "prow"), "pcol"),
        P("pole", "prow", None),
        P("pcol", "pole", None),
        P(),
        P(),
    )
    out_specs = (P("pcol", "pole", "prow"), P("pcol", "pole", None))
    shards = make_shards(mesh.shape["prow"], mesh.shape["pcol"])
    return jax.shard_map(shards, mesh=mesh, in_specs=in_specs, out_specs=out_specs, check_vma=False)
```

```python
import functools

import jax
import jax.numpy as jnp
from jax import lax
from jax.sharding import PartitionSpec as P


def diag_product(values, factor):
    return jnp.einsum("awj,wjb->awb", values, factor, precision=lax.Precision.HIGHEST)


def slot_lookup(positions, slots):
    match = positions[:, None, :] == slots[None, :, None]
    return jnp.argmax(match, axis=2), jnp.any(match, axis=2)


PACKED = (5, 6, 7, 8, 12)


def pack_order(present, size):
    rank = jnp.cumsum(present.astype(jnp.int32), axis=1) - 1
    target = jnp.arange(size, dtype=jnp.int32)
    hit = present[:, None, :] & (rank[:, None, :] == target[None, :, None])
    return jnp.argmax(hit, axis=2).astype(jnp.int32), jnp.any(hit, axis=2)


def make_shards(prow_size, pcol_size):
    def shards(inverse_trailing, factor_blocks, diag_pivots, structure, owner_map):
        width = factor_blocks.shape[2]
        window = factor_blocks.shape[0]
        local_rows = factor_blocks.shape[1]
        owned = inverse_trailing.shape[0] // width
        row_index = lax.axis_index("prow")
        col_index = lax.axis_index("pcol")
        positions = jnp.take(owner_map, structure, axis=0)
        slots = jnp.arange(owned, dtype=jnp.int32)
        segment = local_rows // pcol_size
        mine = lax.dynamic_slice_in_dim(factor_blocks, col_index * segment, segment, axis=1)
        pieces = lax.all_gather(mine, "prow", axis=1, tiled=True)
        count = pieces.shape[1] // segment
        pieces = pieces.reshape(window, count, segment, width)
        windows = jnp.arange(window)
        flat_slots = window * owned
        dest_slots = jnp.arange(pcol_size, dtype=jnp.int32)[:, None] * owned + slots[None, :]
        dest_index, dest_present = jax.vmap(lambda s: slot_lookup(positions, s))(dest_slots)
        dest_index = dest_index.reshape(pcol_size, flat_slots)
        dest_present = dest_present.reshape(pcol_size, flat_slots)
        row_index_map, in_rows = slot_lookup(positions, row_index * owned + slots)
        row_piece = pieces[windows[:, None], row_index_map]
        row_piece = jnp.where(in_rows[..., None, None], row_piece, 0.0)
        row_factor = lax.all_gather(row_piece, "pcol", axis=2, tiled=True)
        row_factor = row_factor.reshape(window, owned * width, width)
        needed = jnp.max(jnp.sum(dest_present.astype(jnp.int32), axis=1))
        branch = jnp.sum((needed > jnp.array(PACKED[:-1], jnp.int32)).astype(jnp.int32))

        def route(size, send):
            received = lax.all_to_all(send[:, :size], "pcol", 0, 0, tiled=True)
            return jnp.pad(received, ((0, 0), (0, flat_slots - size), (0, 0), (0, 0)))

        def reduce_rows(size, chosen):
            part = chosen[:, :size]
            share = part.shape[0] // pcol_size
            part = part.reshape((pcol_size, share) + part.shape[1:])
            summed = jnp.sum(lax.all_to_all(part, "pcol", 0, 0, tiled=True), axis=0)
            return jnp.pad(summed, ((0, 0), (0, flat_slots - size), (0, 0)))

        send_slot, send_valid = pack_order(dest_present, flat_slots)
        send_j = jnp.take_along_axis(dest_index, send_slot, axis=1)
        send = pieces[send_slot // owned, send_j]
        send = jnp.where(send_valid[..., None, None], send, 0.0)
        received = lax.switch(branch, [functools.partial(route, size) for size in PACKED], send)
        blocks = jnp.transpose(received, (1, 0, 2, 3)).reshape(flat_slots, local_rows, width)
        mine = dest_present[col_index]
        rank = jnp.clip(jnp.cumsum(mine.astype(jnp.int32)) - 1, 0, flat_slots - 1)
        col_factor = jnp.where(mine[:, None, None], blocks[rank], 0.0)
        col_factor = col_factor.reshape(window, owned * local_rows, width)
        partial = jnp.einsum("wja,ij->awi", col_factor, inverse_trailing, precision=lax.Precision.HIGHEST)
        partial = partial.reshape(partial.shape[0], flat_slots, width)
        listed = in_rows.reshape(flat_slots)
        pair_slot, _ = pack_order(listed[None, :], flat_slots)
        chosen = jnp.take(partial, pair_slot[0], axis=1)
        summed = lax.switch(branch, [functools.partial(reduce_rows, size) for size in PACKED], chosen)
        pair_rank = jnp.clip(jnp.cumsum(listed.astype(jnp.int32)) - 1, 0, flat_slots - 1)
        rows = jnp.where(listed[None, :, None], -jnp.take(summed, pair_rank, axis=1), 0.0)
        row_inverse = rows.reshape(rows.shape[0], window, owned * width)
        local_diag = diag_product(row_inverse, row_factor)
        gathered = lax.all_gather(local_diag, "prow", axis=0, tiled=False)
        total_diag = jnp.sum(gathered, axis=0)
        diag_inverse = diag_pivots - total_diag
        return (row_inverse, diag_inverse)

    return shards


def solution(mesh):
    in_specs = (
        P(("pole", "prow"), "pcol"),
        P("pole", "prow", None),
        P("pcol", "pole", None),
        P(),
        P(),
    )
    out_specs = (P("pcol", "pole", "prow"), P("pcol", "pole", None))
    shards = make_shards(mesh.shape["prow"], mesh.shape["pcol"])
    return jax.shard_map(shards, mesh=mesh, in_specs=in_specs, out_specs=out_specs, check_vma=False)
```

```python
import functools

import jax
import jax.numpy as jnp
from jax import lax
from jax.sharding import PartitionSpec as P


def diag_product(values, factor):
    return jnp.einsum("awj,wjb->awb", values, factor, precision=lax.Precision.HIGHEST)


def slot_lookup(positions, slots):
    match = positions[:, None, :] == slots[None, :, None]
    return jnp.argmax(match, axis=2), jnp.any(match, axis=2)


PACKED = (6, 8, 12)


def pack_order(present, size):
    rank = jnp.cumsum(present.astype(jnp.int32), axis=1) - 1
    target = jnp.arange(size, dtype=jnp.int32)
    hit = present[:, None, :] & (rank[:, None, :] == target[None, :, None])
    return jnp.argmax(hit, axis=2).astype(jnp.int32), jnp.any(hit, axis=2)


def make_shards(prow_size, pcol_size):
    def shards(inverse_trailing, factor_blocks, diag_pivots, structure, owner_map):
        width = factor_blocks.shape[2]
        window = factor_blocks.shape[0]
        local_rows = factor_blocks.shape[1]
        owned = inverse_trailing.shape[0] // width
        row_index = lax.axis_index("prow")
        col_index = lax.axis_index("pcol")
        positions = jnp.take(owner_map, structure, axis=0)
        slots = jnp.arange(owned, dtype=jnp.int32)
        segment = local_rows // pcol_size
        mine = lax.dynamic_slice_in_dim(factor_blocks, col_index * segment, segment, axis=1)
        pieces = lax.all_gather(mine, "prow", axis=1, tiled=True)
        count = pieces.shape[1] // segment
        pieces = pieces.reshape(window, count, segment, width)
        windows = jnp.arange(window)
        flat_slots = window * owned
        dest_slots = jnp.arange(pcol_size, dtype=jnp.int32)[:, None] * owned + slots[None, :]
        dest_index, dest_present = jax.vmap(lambda s: slot_lookup(positions, s))(dest_slots)
        dest_index = dest_index.reshape(pcol_size, flat_slots)
        dest_present = dest_present.reshape(pcol_size, flat_slots)
        row_index_map, in_rows = slot_lookup(positions, row_index * owned + slots)
        row_piece = pieces[windows[:, None], row_index_map]
        row_piece = jnp.where(in_rows[..., None, None], row_piece, 0.0)
        row_factor = lax.all_gather(row_piece, "pcol", axis=2, tiled=True)
        row_factor = row_factor.reshape(window, owned * width, width)
        needed = jnp.max(jnp.sum(dest_present.astype(jnp.int32), axis=1))
        branch = jnp.sum((needed > jnp.array(PACKED[:-1], jnp.int32)).astype(jnp.int32))

        def route(size, pieces):
            send_slot, send_valid = pack_order(dest_present, size)
            send_w = send_slot // owned
            send_j = jnp.take_along_axis(dest_index, send_slot, axis=1)
            send = pieces[send_w, send_j]
            send = jnp.where(send_valid[..., None, None], send, 0.0)
            received = lax.all_to_all(send, "pcol", 0, 0, tiled=True)
            blocks = jnp.transpose(received, (1, 0, 2, 3)).reshape(size, local_rows, width)
            mine = dest_present[col_index]
            rank = jnp.clip(jnp.cumsum(mine.astype(jnp.int32)) - 1, 0, size - 1)
            return jnp.where(mine[:, None, None], blocks[rank], 0.0)

        def reduce_rows(size, partial):
            pair_slot, _ = pack_order(listed[None, :], size)
            chosen = jnp.take(partial, pair_slot[0], axis=1)
            share = chosen.shape[0] // pcol_size
            chosen = chosen.reshape((pcol_size, share) + chosen.shape[1:])
            summed = jnp.sum(lax.all_to_all(chosen, "pcol", 0, 0, tiled=True), axis=0)
            pair_rank = jnp.clip(jnp.cumsum(listed.astype(jnp.int32)) - 1, 0, size - 1)
            return jnp.where(listed[None, :, None], -jnp.take(summed, pair_rank, axis=1), 0.0)

        listed = in_rows.reshape(flat_slots)
        col_factor = lax.switch(branch, [functools.partial(route, size) for size in PACKED], pieces)
        col_factor = col_factor.reshape(window, owned * local_rows, width)
        partial = jnp.einsum("wja,ij->awi", col_factor, inverse_trailing, precision=lax.Precision.HIGHEST)
        partial = partial.reshape(partial.shape[0], flat_slots, width)
        rows = lax.switch(branch, [functools.partial(reduce_rows, size) for size in PACKED], partial)
        row_inverse = rows.reshape(rows.shape[0], window, owned * width)
        local_diag = diag_product(row_inverse, row_factor)
        gathered = lax.all_gather(local_diag, "prow", axis=0, tiled=False)
        total_diag = jnp.sum(gathered, axis=0)
        diag_inverse = diag_pivots - total_diag
        return (row_inverse, diag_inverse)

    return shards


def solution(mesh):
    in_specs = (
        P(("pole", "prow"), "pcol"),
        P("pole", "prow", None),
        P("pcol", "pole", None),
        P(),
        P(),
    )
    out_specs = (P("pcol", "pole", "prow"), P("pcol", "pole", None))
    shards = make_shards(mesh.shape["prow"], mesh.shape["pcol"])
    return jax.shard_map(shards, mesh=mesh, in_specs=in_specs, out_specs=out_specs, check_vma=False)
```

```python
import functools

import jax
import jax.numpy as jnp
from jax import lax
from jax.sharding import PartitionSpec as P


def diag_product(values, factor):
    return jnp.einsum("awj,wjb->awb", values, factor, precision=lax.Precision.HIGHEST)


def slot_lookup(positions, slots):
    match = positions[:, None, :] == slots[None, :, None]
    return jnp.argmax(match, axis=2), jnp.any(match, axis=2)


PACKED = (6, 8, 12)


def pack_order(present, size):
    rank = jnp.cumsum(present.astype(jnp.int32), axis=1) - 1
    target = jnp.arange(size, dtype=jnp.int32)
    hit = present[:, None, :] & (rank[:, None, :] == target[None, :, None])
    return jnp.argmax(hit, axis=2).astype(jnp.int32), jnp.any(hit, axis=2)


def make_shards(prow_size, pcol_size):
    def shards(inverse_trailing, factor_blocks, diag_pivots, structure, owner_map):
        width = factor_blocks.shape[2]
        window = factor_blocks.shape[0]
        local_rows = factor_blocks.shape[1]
        owned = inverse_trailing.shape[0] // width
        row_index = lax.axis_index("prow")
        col_index = lax.axis_index("pcol")
        positions = jnp.take(owner_map, structure, axis=0)
        slots = jnp.arange(owned, dtype=jnp.int32)
        segment = local_rows // pcol_size
        mine = lax.dynamic_slice_in_dim(factor_blocks, col_index * segment, segment, axis=1)
        pieces = lax.all_gather(mine, "prow", axis=1, tiled=True)
        count = pieces.shape[1] // segment
        pieces = pieces.reshape(window, count, segment, width)
        windows = jnp.arange(window)
        flat_slots = window * owned
        dest_slots = jnp.arange(pcol_size, dtype=jnp.int32)[:, None] * owned + slots[None, :]
        dest_index, dest_present = jax.vmap(lambda s: slot_lookup(positions, s))(dest_slots)
        dest_index = dest_index.reshape(pcol_size, flat_slots)
        dest_present = dest_present.reshape(pcol_size, flat_slots)
        row_index_map, in_rows = slot_lookup(positions, row_index * owned + slots)
        row_piece = pieces[windows[:, None], row_index_map]
        row_piece = jnp.where(in_rows[..., None, None], row_piece, 0.0)
        row_factor = lax.all_gather(row_piece, "pcol", axis=2, tiled=True)
        row_factor = row_factor.reshape(window, owned * width, width)
        needed = jnp.max(jnp.sum(dest_present.astype(jnp.int32), axis=1))
        branch = jnp.sum((needed > jnp.array(PACKED[:-1], jnp.int32)).astype(jnp.int32))

        def route(size, pieces):
            send_slot, send_valid = pack_order(dest_present, size)
            send_w = send_slot // owned
            send_j = jnp.take_along_axis(dest_index, send_slot, axis=1)
            send = pieces[send_w, send_j]
            send = jnp.where(send_valid[..., None, None], send, 0.0)
            received = lax.all_to_all(send, "pcol", 0, 0, tiled=True)
            blocks = jnp.transpose(received, (1, 0, 2, 3)).reshape(size, local_rows, width)
            mine = dest_present[col_index]
            rank = jnp.clip(jnp.cumsum(mine.astype(jnp.int32)) - 1, 0, size - 1)
            return jnp.where(mine[:, None, None], blocks[rank], 0.0)

        def reduce_rows(size, partial):
            pair_slot, _ = pack_order(listed[None, :], size)
            pair_slot = pair_slot[0]
            chosen = partial[pair_slot // owned, :, pair_slot % owned]
            share = chosen.shape[1] // pcol_size
            chosen = chosen.reshape((size, pcol_size, share) + chosen.shape[2:])
            summed = jnp.sum(lax.all_to_all(chosen, "pcol", 1, 1, tiled=True), axis=1)
            pair_rank = jnp.clip(jnp.cumsum(listed.astype(jnp.int32)) - 1, 0, size - 1)
            rows = jnp.where(listed[:, None, None], -jnp.take(summed, pair_rank, axis=0), 0.0)
            return jnp.transpose(rows, (1, 0, 2))

        listed = in_rows.reshape(flat_slots)
        col_factor = lax.switch(branch, [functools.partial(route, size) for size in PACKED], pieces)
        col_factor = col_factor.reshape(window, owned * local_rows, width)
        partial = jnp.einsum("wja,ij->wai", col_factor, inverse_trailing, precision=lax.Precision.HIGHEST)
        partial = partial.reshape(window, partial.shape[1], owned, width)
        rows = lax.switch(branch, [functools.partial(reduce_rows, size) for size in PACKED], partial)
        row_inverse = rows.reshape(rows.shape[0], window, owned * width)
        local_diag = diag_product(row_inverse, row_factor)
        gathered = lax.all_gather(local_diag, "prow", axis=0, tiled=False)
        total_diag = jnp.sum(gathered, axis=0)
        diag_inverse = diag_pivots - total_diag
        return (row_inverse, diag_inverse)

    return shards


def solution(mesh):
    in_specs = (
        P(("pole", "prow"), "pcol"),
        P("pole", "prow", None),
        P("pcol", "pole", None),
        P(),
        P(),
    )
    out_specs = (P("pcol", "pole", "prow"), P("pcol", "pole", None))
    shards = make_shards(mesh.shape["prow"], mesh.shape["pcol"])
    return jax.shard_map(shards, mesh=mesh, in_specs=in_specs, out_specs=out_specs, check_vma=False)
```

```python
import functools

import jax
import jax.numpy as jnp
from jax import lax
from jax.sharding import PartitionSpec as P


def diag_product(values, factor):
    return jnp.einsum("awj,wjb->awb", values, factor, precision=lax.Precision.HIGHEST)


def slot_lookup(positions, slots):
    match = positions[:, None, :] == slots[None, :, None]
    return jnp.argmax(match, axis=2), jnp.any(match, axis=2)


PACKED = (6, 8, 12)


def pack_order(present, size):
    rank = jnp.cumsum(present.astype(jnp.int32), axis=1) - 1
    target = jnp.arange(size, dtype=jnp.int32)
    hit = present[:, None, :] & (rank[:, None, :] == target[None, :, None])
    return jnp.argmax(hit, axis=2).astype(jnp.int32), jnp.any(hit, axis=2)


def make_shards(prow_size, pcol_size):
    def shards(inverse_trailing, factor_blocks, diag_pivots, structure, owner_map):
        width = factor_blocks.shape[2]
        window = factor_blocks.shape[0]
        local_rows = factor_blocks.shape[1]
        owned = inverse_trailing.shape[0] // width
        row_index = lax.axis_index("prow")
        col_index = lax.axis_index("pcol")
        positions = jnp.take(owner_map, structure, axis=0)
        slots = jnp.arange(owned, dtype=jnp.int32)
        segment = local_rows // pcol_size
        mine = lax.dynamic_slice_in_dim(factor_blocks, col_index * segment, segment, axis=1)
        pieces = lax.all_gather(mine, "prow", axis=1, tiled=True)
        count = pieces.shape[1] // segment
        pieces = pieces.reshape(window, count, segment, width)
        windows = jnp.arange(window)
        flat_slots = window * owned
        dest_slots = jnp.arange(pcol_size, dtype=jnp.int32)[:, None] * owned + slots[None, :]
        dest_index, dest_present = jax.vmap(lambda s: slot_lookup(positions, s))(dest_slots)
        dest_index = dest_index.reshape(pcol_size, flat_slots)
        dest_present = dest_present.reshape(pcol_size, flat_slots)
        row_index_map, in_rows = slot_lookup(positions, row_index * owned + slots)
        row_piece = pieces[windows[:, None], row_index_map]
        row_piece = jnp.where(in_rows[..., None, None], row_piece, 0.0)
        row_factor = lax.all_gather(row_piece, "pcol", axis=2, tiled=True)
        row_factor = row_factor.reshape(window, owned * width, width)
        needed = jnp.max(jnp.sum(dest_present.astype(jnp.int32), axis=1))
        branch = jnp.sum((needed > jnp.array(PACKED[:-1], jnp.int32)).astype(jnp.int32))

        full_slot, full_valid = pack_order(dest_present, flat_slots)
        full_j = jnp.take_along_axis(dest_index, full_slot, axis=1)
        listed = in_rows.reshape(flat_slots)
        full_pair, _ = pack_order(listed[None, :], flat_slots)

        def route(size, pieces):
            send_slot, send_valid = full_slot[:, :size], full_valid[:, :size]
            send_w = send_slot // owned
            send_j = full_j[:, :size]
            send = pieces[send_w, send_j]
            send = jnp.where(send_valid[..., None, None], send, 0.0)
            received = lax.all_to_all(send, "pcol", 0, 0, tiled=True)
            blocks = jnp.transpose(received, (1, 0, 2, 3)).reshape(size, local_rows, width)
            mine = dest_present[col_index]
            rank = jnp.clip(jnp.cumsum(mine.astype(jnp.int32)) - 1, 0, size - 1)
            return jnp.where(mine[:, None, None], blocks[rank], 0.0)

        def reduce_rows(size, partial):
            pair_slot = full_pair[0, :size]
            chosen = partial[pair_slot // owned, :, pair_slot % owned]
            share = chosen.shape[1] // pcol_size
            chosen = chosen.reshape((size, pcol_size, share) + chosen.shape[2:])
            summed = jnp.sum(lax.all_to_all(chosen, "pcol", 1, 1, tiled=True), axis=1)
            pair_rank = jnp.clip(jnp.cumsum(listed.astype(jnp.int32)) - 1, 0, size - 1)
            rows = jnp.where(listed[:, None, None], -jnp.take(summed, pair_rank, axis=0), 0.0)
            return jnp.transpose(rows, (1, 0, 2))

        col_factor = lax.switch(branch, [functools.partial(route, size) for size in PACKED], pieces)
        col_factor = col_factor.reshape(window, owned * local_rows, width)
        partial = jnp.einsum("wja,ij->wai", col_factor, inverse_trailing, precision=lax.Precision.HIGHEST)
        partial = partial.reshape(window, partial.shape[1], owned, width)
        rows = lax.switch(branch, [functools.partial(reduce_rows, size) for size in PACKED], partial)
        row_inverse = rows.reshape(rows.shape[0], window, owned * width)
        local_diag = diag_product(row_inverse, row_factor)
        gathered = lax.all_gather(local_diag, "prow", axis=0, tiled=False)
        total_diag = jnp.sum(gathered, axis=0)
        diag_inverse = diag_pivots - total_diag
        return (row_inverse, diag_inverse)

    return shards


def solution(mesh):
    in_specs = (
        P(("pole", "prow"), "pcol"),
        P("pole", "prow", None),
        P("pcol", "pole", None),
        P(),
        P(),
    )
    out_specs = (P("pcol", "pole", "prow"), P("pcol", "pole", None))
    shards = make_shards(mesh.shape["prow"], mesh.shape["pcol"])
    return jax.shard_map(shards, mesh=mesh, in_specs=in_specs, out_specs=out_specs, check_vma=False)
```

```python
import functools

import jax
import jax.numpy as jnp
from jax import lax
from jax.sharding import PartitionSpec as P


def diag_product(values, factor):
    return jnp.einsum("awj,wjb->awb", values, factor, precision=lax.Precision.HIGHEST)


def slot_lookup(positions, slots):
    match = positions[:, None, :] == slots[None, :, None]
    return jnp.argmax(match, axis=2), jnp.any(match, axis=2)


PACKED = (6, 8, 12)


def pack_order(present, size):
    rank = jnp.cumsum(present.astype(jnp.int32), axis=1) - 1
    target = jnp.arange(size, dtype=jnp.int32)
    hit = present[:, None, :] & (rank[:, None, :] == target[None, :, None])
    return jnp.argmax(hit, axis=2).astype(jnp.int32), jnp.any(hit, axis=2)


def make_shards(prow_size, pcol_size):
    def shards(inverse_trailing, factor_blocks, diag_pivots, structure, owner_map):
        width = factor_blocks.shape[2]
        window = factor_blocks.shape[0]
        local_rows = factor_blocks.shape[1]
        owned = inverse_trailing.shape[0] // width
        row_index = lax.axis_index("prow")
        col_index = lax.axis_index("pcol")
        positions = jnp.take(owner_map, structure, axis=0)
        slots = jnp.arange(owned, dtype=jnp.int32)
        segment = local_rows // pcol_size
        mine = lax.dynamic_slice_in_dim(factor_blocks, col_index * segment, segment, axis=1)
        pieces = lax.all_gather(mine, "prow", axis=1, tiled=True)
        count = pieces.shape[1] // segment
        pieces = pieces.reshape(window, count, segment, width)
        windows = jnp.arange(window)
        flat_slots = window * owned
        dest_slots = jnp.arange(pcol_size, dtype=jnp.int32)[:, None] * owned + slots[None, :]
        dest_index, dest_present = jax.vmap(lambda s: slot_lookup(positions, s))(dest_slots)
        dest_index = dest_index.reshape(pcol_size, flat_slots)
        dest_present = dest_present.reshape(pcol_size, flat_slots)
        row_index_map, in_rows = slot_lookup(positions, row_index * owned + slots)
        row_piece = pieces[windows[:, None], row_index_map]
        row_piece = jnp.where(in_rows[..., None, None], row_piece, 0.0)
        row_factor = lax.all_gather(row_piece, "pcol", axis=2, tiled=True)
        row_factor = row_factor.reshape(window, owned * width, width)
        needed = jnp.max(jnp.sum(dest_present.astype(jnp.int32), axis=1))
        branch = jnp.sum((needed > jnp.array(PACKED[:-1], jnp.int32)).astype(jnp.int32))

        def route(size, pieces):
            send_slot, _ = pack_order(dest_present, size)
            send_w = send_slot // owned
            send_j = jnp.take_along_axis(dest_index, send_slot, axis=1)
            send = pieces[send_w, send_j]
            received = lax.all_to_all(send, "pcol", 0, 0, tiled=True)
            blocks = jnp.transpose(received, (1, 0, 2, 3)).reshape(size, local_rows, width)
            mine = dest_present[col_index]
            rank = jnp.clip(jnp.cumsum(mine.astype(jnp.int32)) - 1, 0, size - 1)
            return jnp.where(mine[:, None, None], blocks[rank], 0.0)

        def reduce_rows(size, partial):
            pair_slot, _ = pack_order(listed[None, :], size)
            pair_slot = pair_slot[0]
            chosen = partial[pair_slot // owned, :, pair_slot % owned]
            share = chosen.shape[1] // pcol_size
            chosen = chosen.reshape((size, pcol_size, share) + chosen.shape[2:])
            summed = jnp.sum(lax.all_to_all(chosen, "pcol", 1, 1, tiled=True), axis=1)
            pair_rank = jnp.clip(jnp.cumsum(listed.astype(jnp.int32)) - 1, 0, size - 1)
            rows = jnp.where(listed[:, None, None], -jnp.take(summed, pair_rank, axis=0), 0.0)
            return jnp.transpose(rows, (1, 0, 2))

        listed = in_rows.reshape(flat_slots)
        col_factor = lax.switch(branch, [functools.partial(route, size) for size in PACKED], pieces)
        col_factor = col_factor.reshape(window, owned * local_rows, width)
        partial = jnp.einsum("wja,ij->wai", col_factor, inverse_trailing, precision=lax.Precision.HIGHEST)
        partial = partial.reshape(window, partial.shape[1], owned, width)
        rows = lax.switch(branch, [functools.partial(reduce_rows, size) for size in PACKED], partial)
        row_inverse = rows.reshape(rows.shape[0], window, owned * width)
        local_diag = diag_product(row_inverse, row_factor)
        gathered = lax.all_gather(local_diag, "prow", axis=0, tiled=False)
        total_diag = jnp.sum(gathered, axis=0)
        diag_inverse = diag_pivots - total_diag
        return (row_inverse, diag_inverse)

    return shards


def solution(mesh):
    in_specs = (
        P(("pole", "prow"), "pcol"),
        P("pole", "prow", None),
        P("pcol", "pole", None),
        P(),
        P(),
    )
    out_specs = (P("pcol", "pole", "prow"), P("pcol", "pole", None))
    shards = make_shards(mesh.shape["prow"], mesh.shape["pcol"])
    return jax.shard_map(shards, mesh=mesh, in_specs=in_specs, out_specs=out_specs, check_vma=False)
```

```python
import functools

import jax
import jax.numpy as jnp
from jax import lax
from jax.sharding import PartitionSpec as P


def diag_product(values, factor):
    return jnp.einsum("awj,wjb->awb", values, factor, precision=lax.Precision.HIGHEST)


def slot_lookup(positions, slots):
    match = positions[:, None, :] == slots[None, :, None]
    return jnp.argmax(match, axis=2), jnp.any(match, axis=2)


PACKED = (6, 8, 12)


def pack_order(present, size):
    rank = jnp.cumsum(present.astype(jnp.int32), axis=1) - 1
    target = jnp.arange(size, dtype=jnp.int32)
    hit = present[:, None, :] & (rank[:, None, :] == target[None, :, None])
    return jnp.argmax(hit, axis=2).astype(jnp.int32), jnp.any(hit, axis=2)


def make_shards(prow_size, pcol_size):
    def shards(inverse_trailing, factor_blocks, diag_pivots, structure, owner_map):
        width = factor_blocks.shape[2]
        window = factor_blocks.shape[0]
        local_rows = factor_blocks.shape[1]
        owned = inverse_trailing.shape[0] // width
        row_index = lax.axis_index("prow")
        col_index = lax.axis_index("pcol")
        positions = jnp.take(owner_map, structure, axis=0)
        slots = jnp.arange(owned, dtype=jnp.int32)
        segment = local_rows // pcol_size
        mine = lax.dynamic_slice_in_dim(factor_blocks, col_index * segment, segment, axis=1)
        pieces = lax.all_gather(mine, "prow", axis=1, tiled=True)
        count = pieces.shape[1] // segment
        pieces = pieces.reshape(window, count, segment, width)
        windows = jnp.arange(window)
        flat_slots = window * owned
        dest_slots = jnp.arange(pcol_size, dtype=jnp.int32)[:, None] * owned + slots[None, :]
        dest_index, dest_present = jax.vmap(lambda s: slot_lookup(positions, s))(dest_slots)
        dest_index = dest_index.reshape(pcol_size, flat_slots)
        dest_present = dest_present.reshape(pcol_size, flat_slots)
        row_index_map, in_rows = slot_lookup(positions, row_index * owned + slots)
        row_piece = pieces[windows[:, None], row_index_map]
        row_piece = jnp.where(in_rows[..., None, None], row_piece, 0.0)
        row_factor = lax.all_gather(row_piece, "pcol", axis=2, tiled=True)
        row_factor = row_factor.reshape(window, owned * width, width)
        needed = jnp.max(jnp.sum(dest_present.astype(jnp.int32), axis=1))
        branch = jnp.sum((needed > jnp.array(PACKED[:-1], jnp.int32)).astype(jnp.int32))

        full_slot, _ = pack_order(dest_present, flat_slots)
        full_j = jnp.take_along_axis(dest_index, full_slot, axis=1)
        listed = in_rows.reshape(flat_slots)
        full_pair, _ = pack_order(listed[None, :], flat_slots)

        def route(size, pieces):
            send_slot = full_slot[:, :size]
            send_w = send_slot // owned
            send_j = full_j[:, :size]
            send = pieces[send_w, send_j]
            received = lax.all_to_all(send, "pcol", 0, 0, tiled=True)
            blocks = jnp.transpose(received, (1, 0, 2, 3)).reshape(size, local_rows, width)
            mine = dest_present[col_index]
            rank = jnp.clip(jnp.cumsum(mine.astype(jnp.int32)) - 1, 0, size - 1)
            return jnp.where(mine[:, None, None], blocks[rank], 0.0)

        def reduce_rows(size, partial):
            pair_slot = full_pair[0, :size]
            chosen = partial[pair_slot // owned, :, pair_slot % owned]
            share = chosen.shape[1] // pcol_size
            chosen = chosen.reshape((size, pcol_size, share) + chosen.shape[2:])
            summed = jnp.sum(lax.all_to_all(chosen, "pcol", 1, 1, tiled=True), axis=1)
            pair_rank = jnp.clip(jnp.cumsum(listed.astype(jnp.int32)) - 1, 0, size - 1)
            rows = jnp.where(listed[:, None, None], -jnp.take(summed, pair_rank, axis=0), 0.0)
            return jnp.transpose(rows, (1, 0, 2))

        col_factor = lax.switch(branch, [functools.partial(route, size) for size in PACKED], pieces)
        col_factor = col_factor.reshape(window, owned * local_rows, width)
        partial = jnp.einsum("wja,ij->wai", col_factor, inverse_trailing, precision=lax.Precision.HIGHEST)
        partial = partial.reshape(window, partial.shape[1], owned, width)
        rows = lax.switch(branch, [functools.partial(reduce_rows, size) for size in PACKED], partial)
        row_inverse = rows.reshape(rows.shape[0], window, owned * width)
        local_diag = diag_product(row_inverse, row_factor)
        gathered = lax.all_gather(local_diag, "prow", axis=0, tiled=False)
        total_diag = jnp.sum(gathered, axis=0)
        diag_inverse = diag_pivots - total_diag
        return (row_inverse, diag_inverse)

    return shards


def solution(mesh):
    in_specs = (
        P(("pole", "prow"), "pcol"),
        P("pole", "prow", None),
        P("pcol", "pole", None),
        P(),
        P(),
    )
    out_specs = (P("pcol", "pole", "prow"), P("pcol", "pole", None))
    shards = make_shards(mesh.shape["prow"], mesh.shape["pcol"])
    return jax.shard_map(shards, mesh=mesh, in_specs=in_specs, out_specs=out_specs, check_vma=False)
```

```python
import functools

import jax
import jax.numpy as jnp
from jax import lax
from jax.sharding import PartitionSpec as P


def diag_product(values, factor):
    return jnp.einsum("awj,wjb->awb", values, factor, precision=lax.Precision.HIGHEST)


def slot_lookup(positions, slots):
    match = positions[:, None, :] == slots[None, :, None]
    return jnp.argmax(match, axis=2), jnp.any(match, axis=2)


PACKED = (6, 8, 12)


def pack_order(present, size):
    rank = jnp.cumsum(present.astype(jnp.int32), axis=1) - 1
    target = jnp.arange(size, dtype=jnp.int32)
    hit = present[:, None, :] & (rank[:, None, :] == target[None, :, None])
    return jnp.argmax(hit, axis=2).astype(jnp.int32), jnp.any(hit, axis=2)


def make_shards(prow_size, pcol_size):
    def shards(inverse_trailing, factor_blocks, diag_pivots, structure, owner_map):
        width = factor_blocks.shape[2]
        window = factor_blocks.shape[0]
        local_rows = factor_blocks.shape[1]
        owned = inverse_trailing.shape[0] // width
        row_index = lax.axis_index("prow")
        col_index = lax.axis_index("pcol")
        positions = jnp.take(owner_map, structure, axis=0)
        slots = jnp.arange(owned, dtype=jnp.int32)
        segment = local_rows // pcol_size
        mine = lax.dynamic_slice_in_dim(factor_blocks, col_index * segment, segment, axis=1)
        pieces = lax.all_gather(mine, "prow", axis=1, tiled=True)
        count = pieces.shape[1] // segment
        pieces = pieces.reshape(window, count, segment, width)
        windows = jnp.arange(window)
        flat_slots = window * owned
        dest_slots = jnp.arange(pcol_size, dtype=jnp.int32)[:, None] * owned + slots[None, :]
        dest_index, dest_present = jax.vmap(lambda s: slot_lookup(positions, s))(dest_slots)
        dest_index = dest_index.reshape(pcol_size, flat_slots)
        dest_present = dest_present.reshape(pcol_size, flat_slots)
        row_index_map, in_rows = slot_lookup(positions, row_index * owned + slots)
        row_piece = pieces[windows[:, None], row_index_map]
        row_factor = lax.all_gather(row_piece, "pcol", axis=2, tiled=True)
        row_factor = row_factor.reshape(window, owned * width, width)
        needed = jnp.max(jnp.sum(dest_present.astype(jnp.int32), axis=1))
        branch = jnp.sum((needed > jnp.array(PACKED[:-1], jnp.int32)).astype(jnp.int32))

        def route(size, pieces):
            send_slot, _ = pack_order(dest_present, size)
            send_w = send_slot // owned
            send_j = jnp.take_along_axis(dest_index, send_slot, axis=1)
            send = pieces[send_w, send_j]
            received = lax.all_to_all(send, "pcol", 0, 0, tiled=True)
            blocks = jnp.transpose(received, (1, 0, 2, 3)).reshape(size, local_rows, width)
            mine = dest_present[col_index]
            rank = jnp.clip(jnp.cumsum(mine.astype(jnp.int32)) - 1, 0, size - 1)
            return jnp.where(mine[:, None, None], blocks[rank], 0.0)

        def reduce_rows(size, partial):
            pair_slot, _ = pack_order(listed[None, :], size)
            pair_slot = pair_slot[0]
            chosen = partial[pair_slot // owned, :, pair_slot % owned]
            share = chosen.shape[1] // pcol_size
            chosen = chosen.reshape((size, pcol_size, share) + chosen.shape[2:])
            summed = jnp.sum(lax.all_to_all(chosen, "pcol", 1, 1, tiled=True), axis=1)
            pair_rank = jnp.clip(jnp.cumsum(listed.astype(jnp.int32)) - 1, 0, size - 1)
            rows = jnp.where(listed[:, None, None], -jnp.take(summed, pair_rank, axis=0), 0.0)
            return jnp.transpose(rows, (1, 0, 2))

        listed = in_rows.reshape(flat_slots)
        col_factor = lax.switch(branch, [functools.partial(route, size) for size in PACKED], pieces)
        col_factor = col_factor.reshape(window, owned * local_rows, width)
        partial = jnp.einsum("wja,ij->wai", col_factor, inverse_trailing, precision=lax.Precision.HIGHEST)
        partial = partial.reshape(window, partial.shape[1], owned, width)
        rows = lax.switch(branch, [functools.partial(reduce_rows, size) for size in PACKED], partial)
        row_inverse = rows.reshape(rows.shape[0], window, owned * width)
        local_diag = diag_product(row_inverse, row_factor)
        gathered = lax.all_gather(local_diag, "prow", axis=0, tiled=False)
        total_diag = jnp.sum(gathered, axis=0)
        diag_inverse = diag_pivots - total_diag
        return (row_inverse, diag_inverse)

    return shards


def solution(mesh):
    in_specs = (
        P(("pole", "prow"), "pcol"),
        P("pole", "prow", None),
        P("pcol", "pole", None),
        P(),
        P(),
    )
    out_specs = (P("pcol", "pole", "prow"), P("pcol", "pole", None))
    shards = make_shards(mesh.shape["prow"], mesh.shape["pcol"])
    return jax.shard_map(shards, mesh=mesh, in_specs=in_specs, out_specs=out_specs, check_vma=False)
```
